256 devices in a mesh: seq: 32 (over x, y, core), chan: 4 (over z_hi), rep: 2 (over z_lo).
Axes of the slice: x: 4, y: 4, z: 8 (z_hi: 4, z_lo: 2; z = z_hi * 2 + z_lo), core: 2. Of those that a mesh axis runs over, the one named last changes fastest.
Arguments:
- tokens: bfloat16 [24576, 8192], P(('rep', 'seq'), 'chan'), parts along dimension 0, may hold values from -6 to 6
- w_in: bfloat16 [1024, 3, 8192], P('chan', None, 'seq'), may hold values from -0.0625 to 0.0625
- short_taps: float32 [3, 3, 1024], P(None, None, 'chan'), may hold values from -3 to 3
- decay: float32 [16, 1024], P(None, 'chan'), may hold values from 2.0345053e-05 to 0.03
- residue: float32 [16, 1024], P(None, 'chan'), may hold values from -2 to 2
- skip: float32 [1024], P('chan'), may hold values from -2.5 to 2.5
- w_out: bfloat16 [1024, 8192], P(None, 'chan'), may hold values from -0.1875 to 0.1875
Outputs:
- mixed: bfloat16 [24576, 8192], P(('rep', 'seq'), 'chan'), parts along dimension 0
The draws below stay inside these ranges and needn't reach their ends.
There are 2 independent parts, one for each index of `rep`. The reference program is written for one: setup_inputs(seed, part) draws one part's arguments, and reference() takes and returns one part's arrays. A program takes and returns all parts, laid end to end along the dimension named above; an argument that names none is the same for every part. Nothing has to cross between parts.
All inputs are finite; a program needn't handle non-finite values.
Results may differ from the reference program's by a relative error of at most 0.0079.
Values may be sent and summed in bfloat16 or wider, within the bound.
No kernel may reach another device: no remote copies, remote signals or barrier semaphores. Data moves between devices by JAX's collectives and lax.ppermute only.
A program may use at most 128 MiB of HBM per device.

```python
import math
import jax
import jax.numpy as jnp
from jax import lax

D = 8192
CH = 1024
MODES = 16
KS = 3
TOKENS = 12288


def block_levels(own_key, shape, shards, least, largest):
    factor_of = 1.0
    for axis_at, shards_of in shards:
        draws = jax.random.uniform(jax.random.fold_in(jax.random.fold_in(own_key, 6), axis_at), (shards_of,), jnp.float32, least / len(shards), largest / len(shards))
        factor_of = factor_of * jnp.repeat(jnp.exp(draws), shape[axis_at] // shards_of).reshape((-1,) + (1,) * (len(shape) - 1 - axis_at))
    return factor_of


def gaussian(stream_key, shape, deviation, reach, shards=(), kind=jnp.bfloat16):
    array = deviation * jax.random.normal(stream_key, shape, jnp.float32)
    if shards:
        array = array * block_levels(stream_key, shape, shards, -0.22, 0.18)
    return jnp.clip(array, -reach, reach).astype(kind)


def setup_inputs(seed: int = 0, part: int = 0) -> dict:
    splits = jax.random.split(jax.random.key(seed), 8)
    part_keys = jax.random.split(jax.random.fold_in(splits[7], part), 8)
    tokens = gaussian(part_keys[0], (TOKENS, D), 1.0, 6.0, ((0, 32), (1, 4)))
    w_in = gaussian(splits[1], (CH, 3, D), D ** -0.5, 0.0625, ((0, 4), (2, 32)))
    short_taps = gaussian(splits[2], (KS, 3, CH), 0.6, 3.0, ((2, 4),), jnp.float32)
    decay = jnp.clip(jnp.exp(math.log(0.03) - 7.296115 * jax.random.uniform(splits[3], (MODES, CH), jnp.float32) ** block_levels(splits[3], (MODES, CH), ((1, 4),), -0.2, 0.2)), 2.0345052689663135e-05, 0.03)
    residue = gaussian(splits[4], (MODES, CH), 0.35, 2.0, ((1, 4),), jnp.float32)
    skip = gaussian(splits[5], (CH,), 0.5, 2.5, ((0, 4),), jnp.float32)
    w_out = gaussian(splits[6], (CH, D), CH ** -0.5, 0.1875, ((1, 4),))
    return {"tokens": tokens, "w_in": w_in, "short_taps": short_taps, "decay": decay, "residue": residue, "skip": skip, "w_out": w_out}


def reference(tokens, w_in, short_taps, decay, residue, skip, w_out):
    length = tokens.shape[0]
    channels = w_in.shape[0]
    flat_w = w_in.reshape(channels * 3, w_in.shape[2])
    qkv = jnp.dot(flat_w, tokens.T, preferred_element_type=jnp.float32)
    qkv = qkv.reshape(channels, 3, length).astype(jnp.bfloat16)
    qkv_f = lax.optimization_barrier(qkv).astype(jnp.float32)
    taps_n = short_taps.shape[0]
    padded = jnp.pad(qkv_f, ((0, 0), (0, 0), (taps_n - 1, 0)))
    feat = jnp.zeros((channels, 3, length), jnp.float32)
    for j in range(taps_n):
        tap_j = short_taps[j].astype(jnp.float32).T
        feat = feat + tap_j[:, :, None] * padded[:, :, taps_n - 1 - j:taps_n - 1 - j + length]
    query = feat[:, 0]
    zprod = (feat[:, 1] * feat[:, 2]).astype(jnp.bfloat16)
    z_f = lax.optimization_barrier(zprod).astype(jnp.float32)
    times = jnp.arange(length, dtype=jnp.float32)
    filt = jnp.zeros((channels, length), jnp.float32)
    for m in range(decay.shape[0]):
        rate = decay[m][:, None]
        filt = filt + residue[m][:, None] * jnp.sqrt(rate) * jnp.exp(-rate * times[None, :])
    z_spec = jnp.fft.rfft(z_f, n=2 * length, axis=1)
    h_spec = jnp.fft.rfft(filt, n=2 * length, axis=1)
    conv = jnp.fft.irfft(z_spec * h_spec, n=2 * length, axis=1)[:, :length]
    longc = (conv + skip[:, None] * z_f).astype(jnp.bfloat16)
    long_f = lax.optimization_barrier(longc).astype(jnp.float32)
    gated = (query * long_f).astype(jnp.bfloat16)
    mixed = jnp.dot(gated.T, w_out, preferred_element_type=jnp.float32)
    return mixed.astype(jnp.bfloat16)
```

```python
import math

import jax
import jax.numpy as jnp
from jax import lax
from jax.sharding import PartitionSpec as P


def from_behind(value, axis, steps):
    count = lax.axis_size(axis)
    leading, last = (max(0, -steps), min(count, count - steps))
    return lax.ppermute(value, axis, [(source, source + steps) for source in range(leading, last)])


def hidot(form, left, right):
    return jnp.einsum(
        form, left, right, precision=lax.Precision.HIGHEST, preferred_element_type=jnp.float32
    )


def make_tables(rows_a, cols_b, total_n):
    idx_a = jnp.arange(rows_a, dtype=jnp.int32)
    idx_b = jnp.arange(cols_b, dtype=jnp.int32)
    prod_a = idx_a[:, None] * idx_a[None, :] % rows_a
    ang_a = 2.0 * math.pi / rows_a * prod_a.astype(jnp.float32)
    prod_b = idx_b[:, None] * idx_b[None, :] % cols_b
    ang_b = 2.0 * math.pi / cols_b * prod_b.astype(jnp.float32)
    prod_t = idx_a[:, None] * idx_b[None, :]
    ang_t = 2.0 * math.pi / total_n * prod_t.astype(jnp.float32)
    return (
        jnp.cos(ang_a),
        jnp.sin(ang_a),
        jnp.cos(ang_b),
        jnp.sin(ang_b),
        jnp.cos(ang_t),
        -jnp.sin(ang_t),
    )


def forward_dft(signal, tables):
    cos_a, sin_a, cos_b, sin_b, tw_c, tw_s = tables
    half = signal.shape[1]
    re_one = hidot("ka,pab->pkb", cos_a[:, :half], signal)
    im_one = -hidot("ka,pab->pkb", sin_a[:, :half], signal)
    re_two = re_one * tw_c - im_one * tw_s
    im_two = re_one * tw_s + im_one * tw_c
    spec_re = hidot("pkb,bq->pkq", re_two, cos_b) + hidot("pkb,bq->pkq", im_two, sin_b)
    spec_im = hidot("pkb,bq->pkq", im_two, cos_b) - hidot("pkb,bq->pkq", re_two, sin_b)
    return (spec_re, spec_im)


def inverse_dft(spec_re, spec_im, tables, half, total_n):
    cos_a, sin_a, cos_b, sin_b, tw_c, tw_s = tables
    re_one = hidot("pkq,qb->pkb", spec_re, cos_b) - hidot("pkq,qb->pkb", spec_im, sin_b)
    im_one = hidot("pkq,qb->pkb", spec_re, sin_b) + hidot("pkq,qb->pkb", spec_im, cos_b)
    re_two = re_one * tw_c + im_one * tw_s
    im_two = im_one * tw_c - re_one * tw_s
    out_rows = hidot("ak,pkb->pab", cos_a[:half, :], re_two) - hidot(
        "ak,pkb->pab", sin_a[:half, :], im_two
    )
    return out_rows / total_n


def ring_shift(value, axis, steps):
    count = lax.axis_size(axis)
    return lax.ppermute(value, axis, [(source, (source + steps) % count) for source in range(count)])


def chan_pieces(tokens):
    count = lax.axis_size("chan")
    width = tokens.shape[1]
    if count != 4:
        return [(step, 0, width, ring_shift(tokens, "chan", step)) for step in range(1, count)]
    half = width // 2
    ahead = ring_shift(tokens, "chan", 1)
    behind = ring_shift(tokens, "chan", -1)
    far_lo = ring_shift(ahead[:, :half], "chan", 1)
    far_hi = ring_shift(behind[:, half:], "chan", -1)
    return [(1, 0, width, ahead), (-1, 0, width, behind), (2, 0, half, far_lo), (2, half, width, far_hi)]


def on_device(tokens, w_in, short_taps, decay, residue, skip, w_out):
    seq_count = lax.axis_size("seq")
    seq_rank = lax.axis_index("seq")
    chan_count = lax.axis_size("chan")
    chan_rank = lax.axis_index("chan")
    tok_rows = tokens.shape[0]
    width = tokens.shape[1]
    ch_dev = w_in.shape[0]
    per_dev = ch_dev // seq_count
    w_full = lax.all_gather(w_in, "seq", axis=2, tiled=True)
    w_blocks = w_full.reshape(ch_dev, 3, chan_count, width)

    def block_of(step, lo, hi):
        index = (chan_rank - step) % chan_count
        return lax.dynamic_index_in_dim(w_blocks, index, axis=2, keepdims=False)[:, :, lo:hi]

    qkv = jnp.einsum("cgd,td->cgt", block_of(0, 0, width), tokens, preferred_element_type=jnp.float32)
    for step, lo, hi, piece in chan_pieces(tokens):
        qkv = qkv + jnp.einsum(
            "cgd,td->cgt", block_of(step, lo, hi), piece, preferred_element_type=jnp.float32
        )
    qkv_b = qkv.astype(jnp.bfloat16)
    taps_n = short_taps.shape[0]
    rim_rows = qkv_b[:, :, tok_rows - (taps_n - 1) :]
    prior = from_behind(rim_rows, "seq", 1)
    extended = lax.optimization_barrier(jnp.concatenate([prior, qkv_b], axis=2)).astype(jnp.float32)
    taps = short_taps.transpose(2, 1, 0)
    feat = jnp.zeros((ch_dev, 3, tok_rows), jnp.float32)
    for j in range(taps_n):
        feat = (
            feat
            + taps[:, :, j : j + 1] * extended[:, :, taps_n - 1 - j : taps_n - 1 - j + tok_rows]
        )
    query = feat[:, 0]
    zprod = (feat[:, 1] * feat[:, 2]).astype(jnp.bfloat16)
    whole_seq = lax.all_to_all(
        zprod.reshape(seq_count, per_dev, tok_rows), "seq", split_axis=0, concat_axis=0, tiled=True
    )
    length = tok_rows * seq_count
    total_n = 2 * length
    rows_a = 2 * seq_count
    z_f = lax.optimization_barrier(whole_seq).astype(jnp.float32).transpose(1, 0, 2)
    rates = lax.dynamic_slice_in_dim(decay, seq_rank * per_dev, per_dev, 1)
    weights = lax.dynamic_slice_in_dim(residue, seq_rank * per_dev, per_dev, 1)
    direct = lax.dynamic_slice_in_dim(skip, seq_rank * per_dev, per_dev, 0)
    tables = make_tables(rows_a, tok_rows, total_n)
    z_re, z_im = forward_dft(z_f, tables)
    times = jnp.arange(length, dtype=jnp.float32)
    filt = jnp.zeros((per_dev, length), jnp.float32)
    for m in range(rates.shape[0]):
        rate = rates[m][:, None]
        filt = filt + weights[m][:, None] * jnp.sqrt(rate) * jnp.exp(-rate * times[None, :])
    h_re, h_im = forward_dft(filt.reshape(per_dev, seq_count, tok_rows), tables)
    prod_re = z_re * h_re - z_im * h_im
    prod_im = z_re * h_im + z_im * h_re
    conv = inverse_dft(prod_re, prod_im, tables, seq_count, total_n)
    longc = (conv + direct[:, None, None] * z_f).astype(jnp.bfloat16)
    returned = lax.all_to_all(
        longc.transpose(1, 0, 2), "seq", split_axis=0, concat_axis=0, tiled=True
    )
    long_f = lax.optimization_barrier(returned.reshape(ch_dev, tok_rows)).astype(jnp.float32)
    gated = (query * long_f).astype(jnp.bfloat16)
    mixed = jnp.einsum(
        "ct,ce->te",
        lax.all_gather(gated, "chan", axis=0, tiled=True),
        w_out,
        preferred_element_type=jnp.float32,
    )
    return mixed.astype(jnp.bfloat16)


def solution(mesh):
    placed = (
        P(("rep", "seq"), "chan"),
        P("chan", None, "seq"),
        P(None, None, "chan"),
        P(None, "chan"),
        P(None, "chan"),
        P("chan"),
        P(None, "chan"),
    )
    return jax.shard_map(
        on_device, mesh=mesh, in_specs=placed, out_specs=P(("rep", "seq"), "chan"), check_vma=False
    )
```

```python
import math

import jax
import jax.numpy as jnp
from jax import lax
from jax.sharding import PartitionSpec as P


def from_behind(value, axis, steps):
    count = lax.axis_size(axis)
    leading, last = (max(0, -steps), min(count, count - steps))
    return lax.ppermute(value, axis, [(source, source + steps) for source in range(leading, last)])


def hidot(form, left, right):
    return jnp.einsum(
        form, left, right, precision=lax.Precision.HIGHEST, preferred_element_type=jnp.float32
    )


def make_tables(rows_a, cols_b, total_n):
    idx_a = jnp.arange(rows_a, dtype=jnp.int32)
    idx_b = jnp.arange(cols_b, dtype=jnp.int32)
    prod_a = idx_a[:, None] * idx_a[None, :] % rows_a
    ang_a = 2.0 * math.pi / rows_a * prod_a.astype(jnp.float32)
    prod_b = idx_b[:, None] * idx_b[None, :] % cols_b
    ang_b = 2.0 * math.pi / cols_b * prod_b.astype(jnp.float32)
    prod_t = idx_a[:, None] * idx_b[None, :]
    ang_t = 2.0 * math.pi / total_n * prod_t.astype(jnp.float32)
    return (
        jnp.cos(ang_a),
        jnp.sin(ang_a),
        jnp.cos(ang_b),
        jnp.sin(ang_b),
        jnp.cos(ang_t),
        -jnp.sin(ang_t),
    )


def forward_dft(signal, tables):
    cos_a, sin_a, cos_b, sin_b, tw_c, tw_s = tables
    half = signal.shape[1]
    re_one = hidot("ka,pab->pkb", cos_a[:, :half], signal)
    im_one = -hidot("ka,pab->pkb", sin_a[:, :half], signal)
    re_two = re_one * tw_c - im_one * tw_s
    im_two = re_one * tw_s + im_one * tw_c
    spec_re = hidot("pkb,bq->pkq", re_two, cos_b) + hidot("pkb,bq->pkq", im_two, sin_b)
    spec_im = hidot("pkb,bq->pkq", im_two, cos_b) - hidot("pkb,bq->pkq", re_two, sin_b)
    return (spec_re, spec_im)


def inverse_dft(spec_re, spec_im, tables, half, total_n):
    cos_a, sin_a, cos_b, sin_b, tw_c, tw_s = tables
    re_one = hidot("pkq,qb->pkb", spec_re, cos_b) - hidot("pkq,qb->pkb", spec_im, sin_b)
    im_one = hidot("pkq,qb->pkb", spec_re, sin_b) + hidot("pkq,qb->pkb", spec_im, cos_b)
    re_two = re_one * tw_c + im_one * tw_s
    im_two = im_one * tw_c - re_one * tw_s
    out_rows = hidot("ak,pkb->pab", cos_a[:half, :], re_two) - hidot(
        "ak,pkb->pab", sin_a[:half, :], im_two
    )
    return out_rows / total_n


def ring_shift(value, axis, steps):
    count = lax.axis_size(axis)
    return lax.ppermute(value, axis, [(source, (source + steps) % count) for source in range(count)])


def chan_pieces(tokens):
    count = lax.axis_size("chan")
    width = tokens.shape[1]
    if count != 4:
        return [(step, 0, width, ring_shift(tokens, "chan", step)) for step in range(1, count)]
    half = width // 2
    ahead_lo = ring_shift(tokens[:, :half], "chan", 1)
    behind_hi = ring_shift(tokens[:, half:], "chan", -1)
    far_lo = ring_shift(ahead_lo, "chan", 1)
    far_hi = ring_shift(behind_hi, "chan", -1)
    ahead_hi = ring_shift(tokens[:, half:], "chan", 1)
    behind_lo = ring_shift(tokens[:, :half], "chan", -1)
    return [
        (1, 0, half, ahead_lo),
        (-1, half, width, behind_hi),
        (1, half, width, ahead_hi),
        (-1, 0, half, behind_lo),
        (2, 0, half, far_lo),
        (2, half, width, far_hi),
    ]


def on_device(tokens, w_in, short_taps, decay, residue, skip, w_out):
    seq_count = lax.axis_size("seq")
    seq_rank = lax.axis_index("seq")
    chan_count = lax.axis_size("chan")
    chan_rank = lax.axis_index("chan")
    tok_rows = tokens.shape[0]
    width = tokens.shape[1]
    ch_dev = w_in.shape[0]
    per_dev = ch_dev // seq_count
    w_full = lax.all_gather(w_in, "seq", axis=2, tiled=True)

    def block_of(step, lo, hi):
        index = (chan_rank - step) % chan_count
        return lax.dynamic_slice_in_dim(w_full, index * width + lo, hi - lo, axis=2)

    qkv = jnp.einsum("cgd,td->cgt", block_of(0, 0, width), tokens, preferred_element_type=jnp.float32)
    for step, lo, hi, piece in chan_pieces(tokens):
        qkv = qkv + jnp.einsum(
            "cgd,td->cgt", block_of(step, lo, hi), piece, preferred_element_type=jnp.float32
        )
    qkv_b = qkv.astype(jnp.bfloat16)
    taps_n = short_taps.shape[0]
    rim_rows = qkv_b[:, :, tok_rows - (taps_n - 1) :]
    prior = from_behind(rim_rows, "seq", 1)
    extended = lax.optimization_barrier(jnp.concatenate([prior, qkv_b], axis=2)).astype(jnp.float32)
    taps = short_taps.transpose(2, 1, 0)
    feat = jnp.zeros((ch_dev, 3, tok_rows), jnp.float32)
    for j in range(taps_n):
        feat = (
            feat
            + taps[:, :, j : j + 1] * extended[:, :, taps_n - 1 - j : taps_n - 1 - j + tok_rows]
        )
    query = feat[:, 0]
    zprod = (feat[:, 1] * feat[:, 2]).astype(jnp.bfloat16)
    whole_seq = lax.all_to_all(
        zprod.reshape(seq_count, per_dev, tok_rows), "seq", split_axis=0, concat_axis=0, tiled=True
    )
    length = tok_rows * seq_count
    total_n = 2 * length
    rows_a = 2 * seq_count
    z_f = lax.optimization_barrier(whole_seq).astype(jnp.float32).transpose(1, 0, 2)
    rates = lax.dynamic_slice_in_dim(decay, seq_rank * per_dev, per_dev, 1)
    weights = lax.dynamic_slice_in_dim(residue, seq_rank * per_dev, per_dev, 1)
    direct = lax.dynamic_slice_in_dim(skip, seq_rank * per_dev, per_dev, 0)
    tables = make_tables(rows_a, tok_rows, total_n)
    z_re, z_im = forward_dft(z_f, tables)
    times = jnp.arange(length, dtype=jnp.float32)
    filt = jnp.zeros((per_dev, length), jnp.float32)
    for m in range(rates.shape[0]):
        rate = rates[m][:, None]
        filt = filt + weights[m][:, None] * jnp.sqrt(rate) * jnp.exp(-rate * times[None, :])
    h_re, h_im = forward_dft(filt.reshape(per_dev, seq_count, tok_rows), tables)
    prod_re = z_re * h_re - z_im * h_im
    prod_im = z_re * h_im + z_im * h_re
    conv = inverse_dft(prod_re, prod_im, tables, seq_count, total_n)
    longc = (conv + direct[:, None, None] * z_f).astype(jnp.bfloat16)
    returned = lax.all_to_all(
        longc.transpose(1, 0, 2), "seq", split_axis=0, concat_axis=0, tiled=True
    )
    long_f = lax.optimization_barrier(returned.reshape(ch_dev, tok_rows)).astype(jnp.float32)
    gated = (query * long_f).astype(jnp.bfloat16)
    def rows_of(step):
        index = (chan_rank - step) % chan_count
        return lax.dynamic_slice_in_dim(w_out, index * ch_dev, ch_dev, axis=0)

    shifts = [step if step <= chan_count // 2 else step - chan_count for step in range(1, chan_count)]
    arrived = [(step, ring_shift(gated, "chan", step)) for step in shifts]
    mixed = jnp.einsum("ct,ce->te", gated, rows_of(0), preferred_element_type=jnp.float32)
    for step, piece in arrived:
        mixed = mixed + jnp.einsum(
            "ct,ce->te", piece, rows_of(step), preferred_element_type=jnp.float32
        )
    return mixed.astype(jnp.bfloat16)


def solution(mesh):
    placed = (
        P(("rep", "seq"), "chan"),
        P("chan", None, "seq"),
        P(None, None, "chan"),
        P(None, "chan"),
        P(None, "chan"),
        P("chan"),
        P(None, "chan"),
    )
    return jax.shard_map(
        on_device, mesh=mesh, in_specs=placed, out_specs=P(("rep", "seq"), "chan"), check_vma=False
    )
```

```python
import math

import jax
import jax.numpy as jnp
from jax import lax
from jax.sharding import PartitionSpec as P


def from_behind(value, axis, steps):
    count = lax.axis_size(axis)
    leading, last = (max(0, -steps), min(count, count - steps))
    return lax.ppermute(value, axis, [(source, source + steps) for source in range(leading, last)])


def hidot(form, left, right):
    return jnp.einsum(
        form, left, right, precision=lax.Precision.HIGH, preferred_element_type=jnp.float32
    )


def make_tables(rows_a, cols_b, total_n):
    idx_a = jnp.arange(rows_a, dtype=jnp.int32)
    idx_b = jnp.arange(cols_b, dtype=jnp.int32)
    prod_a = idx_a[:, None] * idx_a[None, :] % rows_a
    ang_a = 2.0 * math.pi / rows_a * prod_a.astype(jnp.float32)
    prod_b = idx_b[:, None] * idx_b[None, :] % cols_b
    ang_b = 2.0 * math.pi / cols_b * prod_b.astype(jnp.float32)
    prod_t = idx_a[:, None] * idx_b[None, :]
    ang_t = 2.0 * math.pi / total_n * prod_t.astype(jnp.float32)
    return (
        jnp.cos(ang_a),
        jnp.sin(ang_a),
        jnp.cos(ang_b),
        jnp.sin(ang_b),
        jnp.cos(ang_t),
        -jnp.sin(ang_t),
    )


def forward_dft(signal, tables):
    cos_a, sin_a, cos_b, sin_b, tw_c, tw_s = tables
    half = signal.shape[1]
    re_one = hidot("ka,pab->pkb", cos_a[:, :half], signal)
    im_one = -hidot("ka,pab->pkb", sin_a[:, :half], signal)
    re_two = re_one * tw_c - im_one * tw_s
    im_two = re_one * tw_s + im_one * tw_c
    spec_re = hidot("pkb,bq->pkq", re_two, cos_b) + hidot("pkb,bq->pkq", im_two, sin_b)
    spec_im = hidot("pkb,bq->pkq", im_two, cos_b) - hidot("pkb,bq->pkq", re_two, sin_b)
    return (spec_re, spec_im)


def inverse_dft(spec_re, spec_im, tables, half, total_n):
    cos_a, sin_a, cos_b, sin_b, tw_c, tw_s = tables
    re_one = hidot("pkq,qb->pkb", spec_re, cos_b) - hidot("pkq,qb->pkb", spec_im, sin_b)
    im_one = hidot("pkq,qb->pkb", spec_re, sin_b) + hidot("pkq,qb->pkb", spec_im, cos_b)
    re_two = re_one * tw_c + im_one * tw_s
    im_two = im_one * tw_c - re_one * tw_s
    out_rows = hidot("ak,pkb->pab", cos_a[:half, :], re_two) - hidot(
        "ak,pkb->pab", sin_a[:half, :], im_two
    )
    return out_rows / total_n


def ring_shift(value, axis, steps):
    count = lax.axis_size(axis)
    return lax.ppermute(value, axis, [(source, (source + steps) % count) for source in range(count)])


def chan_pieces(tokens):
    count = lax.axis_size("chan")
    width = tokens.shape[1]
    if count != 4:
        return [(step, 0, width, ring_shift(tokens, "chan", step)) for step in range(1, count)]
    half = width // 2
    ahead_lo = ring_shift(tokens[:, :half], "chan", 1)
    behind_hi = ring_shift(tokens[:, half:], "chan", -1)
    far_lo = ring_shift(ahead_lo, "chan", 1)
    far_hi = ring_shift(behind_hi, "chan", -1)
    rest_hi, _ = lax.optimization_barrier((tokens[:, half:], ahead_lo))
    rest_lo, _ = lax.optimization_barrier((tokens[:, :half], behind_hi))
    ahead_hi = ring_shift(rest_hi, "chan", 1)
    behind_lo = ring_shift(rest_lo, "chan", -1)
    return [
        (1, 0, half, ahead_lo),
        (-1, half, width, behind_hi),
        (1, half, width, ahead_hi),
        (-1, 0, half, behind_lo),
        (2, 0, half, far_lo),
        (2, half, width, far_hi),
    ]


def on_device(tokens, w_in, short_taps, decay, residue, skip, w_out):
    seq_count = lax.axis_size("seq")
    seq_rank = lax.axis_index("seq")
    chan_count = lax.axis_size("chan")
    chan_rank = lax.axis_index("chan")
    tok_rows = tokens.shape[0]
    width = tokens.shape[1]
    ch_dev = w_in.shape[0]
    per_dev = ch_dev // seq_count
    w_full = lax.all_gather(w_in, "seq", axis=2, tiled=True)

    def block_of(step, lo, hi):
        index = (chan_rank - step) % chan_count
        return lax.dynamic_slice_in_dim(w_full, index * width + lo, hi - lo, axis=2)

    qkv = jnp.einsum("cgd,td->cgt", block_of(0, 0, width), tokens, preferred_element_type=jnp.float32)
    for step, lo, hi, piece in chan_pieces(tokens):
        qkv = qkv + jnp.einsum(
            "cgd,td->cgt", block_of(step, lo, hi), piece, preferred_element_type=jnp.float32
        )
    qkv_b = qkv.astype(jnp.bfloat16)
    taps_n = short_taps.shape[0]
    rim_rows = qkv_b[:, :, tok_rows - (taps_n - 1) :]
    prior = from_behind(rim_rows, "seq", 1)
    extended = lax.optimization_barrier(jnp.concatenate([prior, qkv_b], axis=2)).astype(jnp.float32)
    taps = short_taps.transpose(2, 1, 0)
    feat = jnp.zeros((ch_dev, 3, tok_rows), jnp.float32)
    for j in range(taps_n):
        feat = (
            feat
            + taps[:, :, j : j + 1] * extended[:, :, taps_n - 1 - j : taps_n - 1 - j + tok_rows]
        )
    query = feat[:, 0]
    zprod = (feat[:, 1] * feat[:, 2]).astype(jnp.bfloat16)
    whole_seq = lax.all_to_all(
        zprod.reshape(seq_count, per_dev, tok_rows), "seq", split_axis=0, concat_axis=0, tiled=True
    )
    length = tok_rows * seq_count
    total_n = 2 * length
    rows_a = 2 * seq_count
    z_f = lax.optimization_barrier(whole_seq).astype(jnp.float32).transpose(1, 0, 2)
    rates = lax.dynamic_slice_in_dim(decay, seq_rank * per_dev, per_dev, 1)
    weights = lax.dynamic_slice_in_dim(residue, seq_rank * per_dev, per_dev, 1)
    direct = lax.dynamic_slice_in_dim(skip, seq_rank * per_dev, per_dev, 0)
    tables = make_tables(rows_a, tok_rows, total_n)
    z_re, z_im = forward_dft(z_f, tables)
    times = jnp.arange(length, dtype=jnp.float32)
    filt = jnp.zeros((per_dev, length), jnp.float32)
    for m in range(rates.shape[0]):
        rate = rates[m][:, None]
        filt = filt + weights[m][:, None] * jnp.sqrt(rate) * jnp.exp(-rate * times[None, :])
    h_re, h_im = forward_dft(filt.reshape(per_dev, seq_count, tok_rows), tables)
    prod_re = z_re * h_re - z_im * h_im
    prod_im = z_re * h_im + z_im * h_re
    conv = inverse_dft(prod_re, prod_im, tables, seq_count, total_n)
    longc = (conv + direct[:, None, None] * z_f).astype(jnp.bfloat16)
    returned = lax.all_to_all(
        longc.transpose(1, 0, 2), "seq", split_axis=0, concat_axis=0, tiled=True
    )
    long_f = lax.optimization_barrier(returned.reshape(ch_dev, tok_rows)).astype(jnp.float32)
    gated = (query * long_f).astype(jnp.bfloat16)
    def rows_of(step):
        index = (chan_rank - step) % chan_count
        return lax.dynamic_slice_in_dim(w_out, index * ch_dev, ch_dev, axis=0)

    shifts = [step if step <= chan_count // 2 else step - chan_count for step in range(1, chan_count)]
    arrived = [(step, ring_shift(gated, "chan", step)) for step in shifts]
    mixed = jnp.einsum("ct,ce->te", gated, rows_of(0), preferred_element_type=jnp.float32)
    for step, piece in arrived:
        mixed = mixed + jnp.einsum(
            "ct,ce->te", piece, rows_of(step), preferred_element_type=jnp.float32
        )
    return mixed.astype(jnp.bfloat16)


def solution(mesh):
    placed = (
        P(("rep", "seq"), "chan"),
        P("chan", None, "seq"),
        P(None, None, "chan"),
        P(None, "chan"),
        P(None, "chan"),
        P("chan"),
        P(None, "chan"),
    )
    return jax.shard_map(
        on_device, mesh=mesh, in_specs=placed, out_specs=P(("rep", "seq"), "chan"), check_vma=False
    )
```

```python
import jax
import jax.numpy as jnp
from jax import lax
from jax.sharding import PartitionSpec as P


def from_behind(value, axis, steps):
    count = lax.axis_size(axis)
    leading, last = (max(0, -steps), min(count, count - steps))
    return lax.ppermute(value, axis, [(source, source + steps) for source in range(leading, last)])


def hidot(form, left, right):
    return jnp.einsum(
        form, left, right, precision=lax.Precision.HIGHEST, preferred_element_type=jnp.float32
    )


def ring_shift(value, axis, steps):
    count = lax.axis_size(axis)
    return lax.ppermute(value, axis, [(source, (source + steps) % count) for source in range(count)])


def chan_pieces(tokens):
    count = lax.axis_size("chan")
    width = tokens.shape[1]
    if count != 4:
        return [(step, 0, width, ring_shift(tokens, "chan", step)) for step in range(1, count)]
    half = width // 2
    ahead_lo = ring_shift(tokens[:, :half], "chan", 1)
    behind_hi = ring_shift(tokens[:, half:], "chan", -1)
    far_lo = ring_shift(ahead_lo, "chan", 1)
    far_hi = ring_shift(behind_hi, "chan", -1)
    ahead_hi = ring_shift(tokens[:, half:], "chan", 1)
    behind_lo = ring_shift(tokens[:, :half], "chan", -1)
    return [
        (1, 0, half, ahead_lo),
        (-1, half, width, behind_hi),
        (1, half, width, ahead_hi),
        (-1, 0, half, behind_lo),
        (2, 0, half, far_lo),
        (2, half, width, far_hi),
    ]


def on_device(tokens, w_in, short_taps, decay, residue, skip, w_out):
    seq_count = lax.axis_size("seq")
    seq_rank = lax.axis_index("seq")
    chan_count = lax.axis_size("chan")
    chan_rank = lax.axis_index("chan")
    tok_rows = tokens.shape[0]
    width = tokens.shape[1]
    ch_dev = w_in.shape[0]
    w_full = lax.all_gather(w_in, "seq", axis=2, tiled=True)

    def block_of(step, lo, hi):
        index = (chan_rank - step) % chan_count
        return lax.dynamic_slice_in_dim(w_full, index * width + lo, hi - lo, axis=2)

    qkv = jnp.einsum("cgd,td->cgt", block_of(0, 0, width), tokens, preferred_element_type=jnp.float32)
    for step, lo, hi, piece in chan_pieces(tokens):
        qkv = qkv + jnp.einsum(
            "cgd,td->cgt", block_of(step, lo, hi), piece, preferred_element_type=jnp.float32
        )
    qkv_b = qkv.astype(jnp.bfloat16)
    taps_n = short_taps.shape[0]
    rim_rows = qkv_b[:, :, tok_rows - (taps_n - 1) :]
    prior = from_behind(rim_rows, "seq", 1)
    extended = lax.optimization_barrier(jnp.concatenate([prior, qkv_b], axis=2)).astype(jnp.float32)
    taps = short_taps.transpose(2, 1, 0)
    feat = jnp.zeros((ch_dev, 3, tok_rows), jnp.float32)
    for j in range(taps_n):
        feat = (
            feat
            + taps[:, :, j : j + 1] * extended[:, :, taps_n - 1 - j : taps_n - 1 - j + tok_rows]
        )
    query = feat[:, 0]
    zprod = (feat[:, 1] * feat[:, 2]).astype(jnp.bfloat16)
    z_f = lax.optimization_barrier(zprod).astype(jnp.float32)
    gains = residue * jnp.sqrt(decay)
    tau = jnp.arange(tok_rows, dtype=jnp.float32)
    grow = jnp.exp(decay[:, :, None] * tau)
    fall = jnp.exp(-decay[:, :, None] * tau)
    upper = (tau[:, None] <= tau[None, :]).astype(jnp.float32)
    prefix = hidot("mcs,st->mct", grow * z_f[None], upper)
    intra = fall * prefix
    states = lax.all_gather(intra[:, :, -1], "seq", axis=0, tiled=False)
    blocks = jnp.arange(seq_count)
    lag = jnp.maximum(seq_rank - 1 - blocks, 0).astype(jnp.float32)
    carry = jnp.where(
        (blocks < seq_rank)[:, None, None],
        jnp.exp(-decay[None] * (tok_rows * lag)[:, None, None]),
        0.0,
    )
    incoming = jnp.sum(carry * states, axis=0)
    inter = jnp.exp(-decay[:, :, None] * (tau + 1.0)) * incoming[:, :, None]
    conv = jnp.einsum("mc,mct->ct", gains, intra + inter, precision=lax.Precision.HIGHEST)
    longc = (conv + skip[:, None] * z_f).astype(jnp.bfloat16)
    long_f = lax.optimization_barrier(longc).astype(jnp.float32)
    gated = (query * long_f).astype(jnp.bfloat16)
    def rows_of(step):
        index = (chan_rank - step) % chan_count
        return lax.dynamic_slice_in_dim(w_out, index * ch_dev, ch_dev, axis=0)

    shifts = [step if step <= chan_count // 2 else step - chan_count for step in range(1, chan_count)]
    arrived = [(step, ring_shift(gated, "chan", step)) for step in shifts]
    mixed = jnp.einsum("ct,ce->te", gated, rows_of(0), preferred_element_type=jnp.float32)
    for step, piece in arrived:
        mixed = mixed + jnp.einsum(
            "ct,ce->te", piece, rows_of(step), preferred_element_type=jnp.float32
        )
    return mixed.astype(jnp.bfloat16)


def solution(mesh):
    placed = (
        P(("rep", "seq"), "chan"),
        P("chan", None, "seq"),
        P(None, None, "chan"),
        P(None, "chan"),
        P(None, "chan"),
        P("chan"),
        P(None, "chan"),
    )
    return jax.shard_map(
        on_device, mesh=mesh, in_specs=placed, out_specs=P(("rep", "seq"), "chan"), check_vma=False
    )
```

```python
import jax
import jax.numpy as jnp
from jax import lax
from jax.sharding import PartitionSpec as P


def from_behind(value, axis, steps):
    count = lax.axis_size(axis)
    leading, last = (max(0, -steps), min(count, count - steps))
    return lax.ppermute(value, axis, [(source, source + steps) for source in range(leading, last)])


def hidot(form, left, right):
    return jnp.einsum(
        form, left, right, precision=lax.Precision.HIGHEST, preferred_element_type=jnp.float32
    )


def ring_shift(value, axis, steps):
    count = lax.axis_size(axis)
    return lax.ppermute(value, axis, [(source, (source + steps) % count) for source in range(count)])


def chan_pieces(tokens):
    count = lax.axis_size("chan")
    width = tokens.shape[1]
    if count != 4:
        return [(step, 0, width, ring_shift(tokens, "chan", step)) for step in range(1, count)]
    half = width // 2
    ahead_lo = ring_shift(tokens[:, :half], "chan", 1)
    behind_hi = ring_shift(tokens[:, half:], "chan", -1)
    far_lo = ring_shift(ahead_lo, "chan", 1)
    far_hi = ring_shift(behind_hi, "chan", -1)
    ahead_hi = ring_shift(tokens[:, half:], "chan", 1)
    behind_lo = ring_shift(tokens[:, :half], "chan", -1)
    return [
        (1, 0, half, ahead_lo),
        (-1, half, width, behind_hi),
        (1, half, width, ahead_hi),
        (-1, 0, half, behind_lo),
        (2, 0, half, far_lo),
        (2, half, width, far_hi),
    ]


def on_device(tokens, w_in, short_taps, decay, residue, skip, w_out):
    seq_count = lax.axis_size("seq")
    seq_rank = lax.axis_index("seq")
    chan_count = lax.axis_size("chan")
    chan_rank = lax.axis_index("chan")
    tok_rows = tokens.shape[0]
    width = tokens.shape[1]
    ch_dev = w_in.shape[0]
    w_full = lax.all_gather(w_in, "seq", axis=2, tiled=True)

    def block_of(step, lo, hi):
        index = (chan_rank - step) % chan_count
        return lax.dynamic_slice_in_dim(w_full, index * width + lo, hi - lo, axis=2)

    qkv = jnp.einsum("cgd,td->cgt", block_of(0, 0, width), tokens, preferred_element_type=jnp.float32)
    for step, lo, hi, piece in chan_pieces(tokens):
        qkv = qkv + jnp.einsum(
            "cgd,td->cgt", block_of(step, lo, hi), piece, preferred_element_type=jnp.float32
        )
    qkv_b = qkv.astype(jnp.bfloat16)
    taps_n = short_taps.shape[0]
    rim_rows = qkv_b[:, :, tok_rows - (taps_n - 1) :]
    prior = from_behind(rim_rows, "seq", 1)
    extended = lax.optimization_barrier(jnp.concatenate([prior, qkv_b], axis=2)).astype(jnp.float32)
    taps = short_taps.transpose(2, 1, 0)
    feat = jnp.zeros((ch_dev, 3, tok_rows), jnp.float32)
    for j in range(taps_n):
        feat = (
            feat
            + taps[:, :, j : j + 1] * extended[:, :, taps_n - 1 - j : taps_n - 1 - j + tok_rows]
        )
    query = feat[:, 0]
    zprod = (feat[:, 1] * feat[:, 2]).astype(jnp.bfloat16)
    z_f = lax.optimization_barrier(zprod).astype(jnp.float32)
    gains = residue * jnp.sqrt(decay)
    tau = jnp.arange(tok_rows, dtype=jnp.float32)
    grow = jnp.exp(decay[:, :, None] * tau)
    fall = jnp.exp(-decay[:, :, None] * tau)
    upper = (tau[:, None] <= tau[None, :]).astype(jnp.float32)
    tail = jnp.exp(-decay[:, :, None] * (tok_rows - 1.0 - tau))
    ending = jnp.sum(tail * z_f[None], axis=2)
    blocks = jnp.arange(seq_count)
    lag = jnp.maximum(blocks - 1 - seq_rank, 0).astype(jnp.float32)
    carry = jnp.where(
        (blocks > seq_rank)[:, None, None],
        jnp.exp(-decay[None] * (tok_rows * lag)[:, None, None]),
        0.0,
    )
    incoming = lax.psum_scatter(carry * ending[None], "seq", scatter_dimension=0, tiled=True)[0]
    prefix = hidot("mcs,st->mct", grow * z_f[None], upper)
    intra = fall * prefix
    inter = jnp.exp(-decay[:, :, None] * (tau + 1.0)) * incoming[:, :, None]
    conv = jnp.einsum("mc,mct->ct", gains, intra + inter, precision=lax.Precision.HIGHEST)
    longc = (conv + skip[:, None] * z_f).astype(jnp.bfloat16)
    long_f = lax.optimization_barrier(longc).astype(jnp.float32)
    gated = (query * long_f).astype(jnp.bfloat16)
    def rows_of(step):
        index = (chan_rank - step) % chan_count
        return lax.dynamic_slice_in_dim(w_out, index * ch_dev, ch_dev, axis=0)

    shifts = [step if step <= chan_count // 2 else step - chan_count for step in range(1, chan_count)]
    arrived = [(step, ring_shift(gated, "chan", step)) for step in shifts]
    mixed = jnp.einsum("ct,ce->te", gated, rows_of(0), preferred_element_type=jnp.float32)
    for step, piece in arrived:
        mixed = mixed + jnp.einsum(
            "ct,ce->te", piece, rows_of(step), preferred_element_type=jnp.float32
        )
    return mixed.astype(jnp.bfloat16)


def solution(mesh):
    placed = (
        P(("rep", "seq"), "chan"),
        P("chan", None, "seq"),
        P(None, None, "chan"),
        P(None, "chan"),
        P(None, "chan"),
        P("chan"),
        P(None, "chan"),
    )
    return jax.shard_map(
        on_device, mesh=mesh, in_specs=placed, out_specs=P(("rep", "seq"), "chan"), check_vma=False
    )
```

```python
import jax
import jax.numpy as jnp
from jax import lax
from jax.sharding import PartitionSpec as P


def from_behind(value, axis, steps):
    count = lax.axis_size(axis)
    leading, last = (max(0, -steps), min(count, count - steps))
    return lax.ppermute(value, axis, [(source, source + steps) for source in range(leading, last)])


def hidot(form, left, right):
    return jnp.einsum(
        form, left, right, precision=lax.Precision.HIGHEST, preferred_element_type=jnp.float32
    )


def ring_shift(value, axis, steps):
    count = lax.axis_size(axis)
    return lax.ppermute(value, axis, [(source, (source + steps) % count) for source in range(count)])


def chan_pieces(tokens):
    count = lax.axis_size("chan")
    width = tokens.shape[1]
    if count != 4:
        return [(step, 0, width, ring_shift(tokens, "chan", step)) for step in range(1, count)]
    half = width // 2
    ahead_lo = ring_shift(tokens[:, :half], "chan", 1)
    behind_hi = ring_shift(tokens[:, half:], "chan", -1)
    far_lo = ring_shift(ahead_lo, "chan", 1)
    far_hi = ring_shift(behind_hi, "chan", -1)
    ahead_hi = ring_shift(tokens[:, half:], "chan", 1)
    behind_lo = ring_shift(tokens[:, :half], "chan", -1)
    return [
        (1, 0, half, ahead_lo),
        (-1, half, width, behind_hi),
        (1, half, width, ahead_hi),
        (-1, 0, half, behind_lo),
        (2, 0, half, far_lo),
        (2, half, width, far_hi),
    ]


def on_device(tokens, w_in, short_taps, decay, residue, skip, w_out):
    seq_count = lax.axis_size("seq")
    seq_rank = lax.axis_index("seq")
    chan_count = lax.axis_size("chan")
    chan_rank = lax.axis_index("chan")
    tok_rows = tokens.shape[0]
    width = tokens.shape[1]
    ch_dev = w_in.shape[0]
    w_full = lax.all_gather(w_in, "seq", axis=2, tiled=True)

    def block_of(step, lo, hi):
        index = (chan_rank - step) % chan_count
        return lax.dynamic_slice_in_dim(w_full, index * width + lo, hi - lo, axis=2)

    qkv = jnp.einsum("cgd,td->cgt", block_of(0, 0, width), tokens, preferred_element_type=jnp.float32)
    for step, lo, hi, piece in chan_pieces(tokens):
        qkv = qkv + jnp.einsum(
            "cgd,td->cgt", block_of(step, lo, hi), piece, preferred_element_type=jnp.float32
        )
    qkv_b = qkv.astype(jnp.bfloat16)
    taps_n = short_taps.shape[0]
    rim_rows = qkv_b[:, :, tok_rows - (taps_n - 1) :]
    prior = from_behind(rim_rows, "seq", 1)
    extended = lax.optimization_barrier(jnp.concatenate([prior, qkv_b], axis=2)).astype(jnp.float32)
    taps = short_taps.transpose(2, 1, 0)
    feat = jnp.zeros((ch_dev, 3, tok_rows), jnp.float32)
    for j in range(taps_n):
        feat = (
            feat
            + taps[:, :, j : j + 1] * extended[:, :, taps_n - 1 - j : taps_n - 1 - j + tok_rows]
        )
    query = feat[:, 0]
    zprod = (feat[:, 1] * feat[:, 2]).astype(jnp.bfloat16)
    z_f = lax.optimization_barrier(zprod).astype(jnp.float32)
    gains = residue * jnp.sqrt(decay)
    tau = jnp.arange(tok_rows, dtype=jnp.float32)
    grow = jnp.exp(decay[:, :, None] * tau)
    fall = jnp.exp(-decay[:, :, None] * tau)
    upper = (tau[:, None] <= tau[None, :]).astype(jnp.float32)
    tail = jnp.exp(-decay[:, :, None] * (tok_rows - 1.0 - tau))
    ending = jnp.sum(tail * z_f[None], axis=2)
    states = lax.all_to_all(
        jnp.broadcast_to(ending[None], (seq_count,) + ending.shape),
        "seq",
        split_axis=0,
        concat_axis=0,
        tiled=True,
    )
    blocks = jnp.arange(seq_count)
    lag = jnp.maximum(seq_rank - 1 - blocks, 0).astype(jnp.float32)
    carry = jnp.where(
        (blocks < seq_rank)[:, None, None],
        jnp.exp(-decay[None] * (tok_rows * lag)[:, None, None]),
        0.0,
    )
    incoming = jnp.sum(carry * states, axis=0)
    prefix = hidot("mcs,st->mct", grow * z_f[None], upper)
    intra = fall * prefix
    inter = jnp.exp(-decay[:, :, None] * (tau + 1.0)) * incoming[:, :, None]
    conv = jnp.einsum("mc,mct->ct", gains, intra + inter, precision=lax.Precision.HIGHEST)
    longc = (conv + skip[:, None] * z_f).astype(jnp.bfloat16)
    long_f = lax.optimization_barrier(longc).astype(jnp.float32)
    gated = (query * long_f).astype(jnp.bfloat16)
    def rows_of(step):
        index = (chan_rank - step) % chan_count
        return lax.dynamic_slice_in_dim(w_out, index * ch_dev, ch_dev, axis=0)

    shifts = [step if step <= chan_count // 2 else step - chan_count for step in range(1, chan_count)]
    arrived = [(step, ring_shift(gated, "chan", step)) for step in shifts]
    mixed = jnp.einsum("ct,ce->te", gated, rows_of(0), preferred_element_type=jnp.float32)
    for step, piece in arrived:
        mixed = mixed + jnp.einsum(
            "ct,ce->te", piece, rows_of(step), preferred_element_type=jnp.float32
        )
    return mixed.astype(jnp.bfloat16)


def solution(mesh):
    placed = (
        P(("rep", "seq"), "chan"),
        P("chan", None, "seq"),
        P(None, None, "chan"),
        P(None, "chan"),
        P(None, "chan"),
        P("chan"),
        P(None, "chan"),
    )
    return jax.shard_map(
        on_device, mesh=mesh, in_specs=placed, out_specs=P(("rep", "seq"), "chan"), check_vma=False
    )
```

```python
import jax
import jax.numpy as jnp
from jax import lax
from jax.sharding import PartitionSpec as P


def from_behind(value, axis, steps):
    count = lax.axis_size(axis)
    leading, last = (max(0, -steps), min(count, count - steps))
    return lax.ppermute(value, axis, [(source, source + steps) for source in range(leading, last)])


def hidot(form, left, right):
    return jnp.einsum(
        form, left, right, precision=lax.Precision.HIGHEST, preferred_element_type=jnp.float32
    )


def ring_shift(value, axis, steps):
    count = lax.axis_size(axis)
    return lax.ppermute(value, axis, [(source, (source + steps) % count) for source in range(count)])


def chan_pieces(tokens):
    count = lax.axis_size("chan")
    width = tokens.shape[1]
    if count != 4:
        return [(step, 0, width, ring_shift(tokens, "chan", step)) for step in range(1, count)]
    half = width // 2
    ahead_lo = ring_shift(tokens[:, :half], "chan", 1)
    behind_hi = ring_shift(tokens[:, half:], "chan", -1)
    far_lo = ring_shift(ahead_lo, "chan", 1)
    far_hi = ring_shift(behind_hi, "chan", -1)
    ahead_hi = ring_shift(tokens[:, half:], "chan", 1)
    behind_lo = ring_shift(tokens[:, :half], "chan", -1)
    return [
        (1, 0, half, ahead_lo),
        (-1, half, width, behind_hi),
        (1, half, width, ahead_hi),
        (-1, 0, half, behind_lo),
        (2, 0, half, far_lo),
        (2, half, width, far_hi),
    ]


def on_device(tokens, w_in, short_taps, decay, residue, skip, w_out):
    seq_count = lax.axis_size("seq")
    seq_rank = lax.axis_index("seq")
    chan_count = lax.axis_size("chan")
    chan_rank = lax.axis_index("chan")
    tok_rows = tokens.shape[0]
    width = tokens.shape[1]
    ch_dev = w_in.shape[0]
    w_full = lax.all_gather(w_in, "seq", axis=2, tiled=True)

    def block_of(step, lo, hi):
        index = (chan_rank - step) % chan_count
        return lax.dynamic_slice_in_dim(w_full, index * width + lo, hi - lo, axis=2)

    qkv = jnp.einsum("cgd,td->cgt", block_of(0, 0, width), tokens, preferred_element_type=jnp.float32)
    for step, lo, hi, piece in chan_pieces(tokens):
        qkv = qkv + jnp.einsum(
            "cgd,td->cgt", block_of(step, lo, hi), piece, preferred_element_type=jnp.float32
        )
    qkv_b = qkv.astype(jnp.bfloat16)
    taps_n = short_taps.shape[0]
    rim_rows = qkv_b[:, :, tok_rows - (taps_n - 1) :]
    prior = from_behind(rim_rows, "seq", 1)
    extended = lax.optimization_barrier(jnp.concatenate([prior, qkv_b], axis=2)).astype(jnp.float32)
    taps = short_taps.transpose(2, 1, 0)
    feat = jnp.zeros((ch_dev, 3, tok_rows), jnp.float32)
    for j in range(taps_n):
        feat = (
            feat
            + taps[:, :, j : j + 1] * extended[:, :, taps_n - 1 - j : taps_n - 1 - j + tok_rows]
        )
    query = feat[:, 0]
    zprod = (feat[:, 1] * feat[:, 2]).astype(jnp.bfloat16)
    z_f = lax.optimization_barrier(zprod).astype(jnp.float32)
    gains = residue * jnp.sqrt(decay)
    tau = jnp.arange(tok_rows, dtype=jnp.float32)
    grow = jnp.exp(decay[:, :, None] * tau)
    fall = jnp.exp(-decay[:, :, None] * tau)
    upper = (tau[:, None] <= tau[None, :]).astype(jnp.float32)
    tail = jnp.exp(-decay[:, :, None] * (tok_rows - 1.0 - tau))
    ending = jnp.sum(tail * z_f[None], axis=2)
    states = lax.all_to_all(
        jnp.broadcast_to(ending[None], (seq_count,) + ending.shape),
        "seq",
        split_axis=0,
        concat_axis=0,
        tiled=True,
    )
    blocks = jnp.arange(seq_count)
    lag = jnp.maximum(seq_rank - 1 - blocks, 0).astype(jnp.float32)
    carry = jnp.where(
        (blocks < seq_rank)[:, None, None],
        jnp.exp(-decay[None] * (tok_rows * lag)[:, None, None]),
        0.0,
    )
    incoming = jnp.sum(carry * states, axis=0)
    prefix = hidot("mcs,st->mct", grow * z_f[None], upper)
    intra = fall * prefix
    near = jnp.sum(gains[:, :, None] * intra, axis=0)
    onward = lax.optimization_barrier(jnp.exp(-decay[:, :, None] * (tau + 1.0)))
    conv = near + jnp.sum((gains * incoming)[:, :, None] * onward, axis=0)
    longc = (conv + skip[:, None] * z_f).astype(jnp.bfloat16)
    long_f = lax.optimization_barrier(longc).astype(jnp.float32)
    gated = (query * long_f).astype(jnp.bfloat16)
    def rows_of(step):
        index = (chan_rank - step) % chan_count
        return lax.dynamic_slice_in_dim(w_out, index * ch_dev, ch_dev, axis=0)

    shifts = [step if step <= chan_count // 2 else step - chan_count for step in range(1, chan_count)]
    arrived = [(step, ring_shift(gated, "chan", step)) for step in shifts]
    mixed = jnp.einsum("ct,ce->te", gated, rows_of(0), preferred_element_type=jnp.float32)
    for step, piece in arrived:
        mixed = mixed + jnp.einsum(
            "ct,ce->te", piece, rows_of(step), preferred_element_type=jnp.float32
        )
    return mixed.astype(jnp.bfloat16)


def solution(mesh):
    placed = (
        P(("rep", "seq"), "chan"),
        P("chan", None, "seq"),
        P(None, None, "chan"),
        P(None, "chan"),
        P(None, "chan"),
        P("chan"),
        P(None, "chan"),
    )
    return jax.shard_map(
        on_device, mesh=mesh, in_specs=placed, out_specs=P(("rep", "seq"), "chan"), check_vma=False
    )
```

```python
import jax
import jax.numpy as jnp
from jax import lax
from jax.sharding import PartitionSpec as P


def from_behind(value, axis, steps):
    count = lax.axis_size(axis)
    leading, last = (max(0, -steps), min(count, count - steps))
    return lax.ppermute(value, axis, [(source, source + steps) for source in range(leading, last)])


def hidot(form, left, right):
    return jnp.einsum(
        form, left, right, precision=lax.Precision.HIGHEST, preferred_element_type=jnp.float32
    )


def ring_shift(value, axis, steps):
    count = lax.axis_size(axis)
    return lax.ppermute(value, axis, [(source, (source + steps) % count) for source in range(count)])


def chan_pieces(tokens):
    count = lax.axis_size("chan")
    width = tokens.shape[1]
    if count != 4:
        return [(step, 0, width, ring_shift(tokens, "chan", step)) for step in range(1, count)]
    half = width // 2
    ahead_lo = ring_shift(tokens[:, :half], "chan", 1)
    behind_hi = ring_shift(tokens[:, half:], "chan", -1)
    far_lo = ring_shift(ahead_lo, "chan", 1)
    far_hi = ring_shift(behind_hi, "chan", -1)
    ahead_hi = ring_shift(tokens[:, half:], "chan", 1)
    behind_lo = ring_shift(tokens[:, :half], "chan", -1)
    return [
        (1, 0, half, ahead_lo),
        (-1, half, width, behind_hi),
        (1, half, width, ahead_hi),
        (-1, 0, half, behind_lo),
        (2, 0, half, far_lo),
        (2, half, width, far_hi),
    ]


def on_device(tokens, w_in, short_taps, decay, residue, skip, w_out):
    seq_count = lax.axis_size("seq")
    seq_rank = lax.axis_index("seq")
    chan_count = lax.axis_size("chan")
    chan_rank = lax.axis_index("chan")
    tok_rows = tokens.shape[0]
    width = tokens.shape[1]
    ch_dev = w_in.shape[0]
    w_full = lax.all_gather(w_in, "seq", axis=2, tiled=True)

    def block_of(step, lo, hi):
        index = (chan_rank - step) % chan_count
        return lax.dynamic_slice_in_dim(w_full, index * width + lo, hi - lo, axis=2)

    qkv = jnp.einsum("cgd,td->cgt", block_of(0, 0, width), tokens, preferred_element_type=jnp.float32)
    for step, lo, hi, piece in chan_pieces(tokens):
        qkv = qkv + jnp.einsum(
            "cgd,td->cgt", block_of(step, lo, hi), piece, preferred_element_type=jnp.float32
        )
    qkv_b = qkv.astype(jnp.bfloat16)
    taps_n = short_taps.shape[0]
    rim_rows = qkv_b[:, :, tok_rows - (taps_n - 1) :]
    prior = from_behind(rim_rows, "seq", 1)
    extended = lax.optimization_barrier(jnp.concatenate([prior, qkv_b], axis=2)).astype(jnp.float32)
    taps = short_taps.transpose(2, 1, 0)
    feat = jnp.zeros((ch_dev, 3, tok_rows), jnp.float32)
    for j in range(taps_n):
        feat = (
            feat
            + taps[:, :, j : j + 1] * extended[:, :, taps_n - 1 - j : taps_n - 1 - j + tok_rows]
        )
    query = feat[:, 0]
    zprod = (feat[:, 1] * feat[:, 2]).astype(jnp.bfloat16)
    z_f = lax.optimization_barrier(zprod).astype(jnp.float32)
    gains = residue * jnp.sqrt(decay)
    tau = jnp.arange(tok_rows, dtype=jnp.float32)
    grow = jnp.exp(decay[:, :, None] * tau)
    fall = jnp.exp(-decay[:, :, None] * tau)
    upper = (tau[:, None] <= tau[None, :]).astype(jnp.float32)
    tail = jnp.exp(-decay[:, :, None] * (tok_rows - 1.0 - tau))
    ending = jnp.sum(tail * z_f[None], axis=2)
    incoming = from_behind(ending, "seq", 1)
    span = 1
    while span < seq_count:
        incoming = incoming + jnp.exp(-decay * float(tok_rows * span)) * from_behind(incoming, "seq", span)
        span *= 2
    prefix = hidot("mcs,st->mct", grow * z_f[None], upper)
    intra = fall * prefix
    near = jnp.sum(gains[:, :, None] * intra, axis=0)
    onward = lax.optimization_barrier(jnp.exp(-decay[:, :, None] * (tau + 1.0)))
    conv = near + jnp.sum((gains * incoming)[:, :, None] * onward, axis=0)
    longc = (conv + skip[:, None] * z_f).astype(jnp.bfloat16)
    long_f = lax.optimization_barrier(longc).astype(jnp.float32)
    gated = (query * long_f).astype(jnp.bfloat16)
    def rows_of(step):
        index = (chan_rank - step) % chan_count
        return lax.dynamic_slice_in_dim(w_out, index * ch_dev, ch_dev, axis=0)

    shifts = [step if step <= chan_count // 2 else step - chan_count for step in range(1, chan_count)]
    arrived = [(step, ring_shift(gated, "chan", step)) for step in shifts]
    mixed = jnp.einsum("ct,ce->te", gated, rows_of(0), preferred_element_type=jnp.float32)
    for step, piece in arrived:
        mixed = mixed + jnp.einsum(
            "ct,ce->te", piece, rows_of(step), preferred_element_type=jnp.float32
        )
    return mixed.astype(jnp.bfloat16)


def solution(mesh):
    placed = (
        P(("rep", "seq"), "chan"),
        P("chan", None, "seq"),
        P(None, None, "chan"),
        P(None, "chan"),
        P(None, "chan"),
        P("chan"),
        P(None, "chan"),
    )
    return jax.shard_map(
        on_device, mesh=mesh, in_specs=placed, out_specs=P(("rep", "seq"), "chan"), check_vma=False
    )
```

```python
import jax
import jax.numpy as jnp
from jax import lax
from jax.sharding import PartitionSpec as P


def from_behind(value, axis, steps):
    count = lax.axis_size(axis)
    leading, last = (max(0, -steps), min(count, count - steps))
    return lax.ppermute(value, axis, [(source, source + steps) for source in range(leading, last)])


def hidot(form, left, right):
    return jnp.einsum(
        form, left, right, precision=lax.Precision.HIGHEST, preferred_element_type=jnp.float32
    )


def ring_shift(value, axis, steps):
    count = lax.axis_size(axis)
    return lax.ppermute(value, axis, [(source, (source + steps) % count) for source in range(count)])


def chan_pieces(tokens):
    count = lax.axis_size("chan")
    width = tokens.shape[1]
    if count != 4:
        return [(step, 0, width, ring_shift(tokens, "chan", step)) for step in range(1, count)]
    half = width // 2
    ahead_lo = ring_shift(tokens[:, :half], "chan", 1)
    behind_hi = ring_shift(tokens[:, half:], "chan", -1)
    far_lo = ring_shift(ahead_lo, "chan", 1)
    far_hi = ring_shift(behind_hi, "chan", -1)
    ahead_hi = ring_shift(tokens[:, half:], "chan", 1)
    behind_lo = ring_shift(tokens[:, :half], "chan", -1)
    return [
        (1, 0, half, ahead_lo),
        (-1, half, width, behind_hi),
        (1, half, width, ahead_hi),
        (-1, 0, half, behind_lo),
        (2, 0, half, far_lo),
        (2, half, width, far_hi),
    ]


def on_device(tokens, w_in, short_taps, decay, residue, skip, w_out):
    seq_count = lax.axis_size("seq")
    seq_rank = lax.axis_index("seq")
    chan_count = lax.axis_size("chan")
    chan_rank = lax.axis_index("chan")
    tok_rows = tokens.shape[0]
    width = tokens.shape[1]
    ch_dev = w_in.shape[0]
    w_full = lax.all_gather(w_in, "seq", axis=2, tiled=True)

    def block_of(step, lo, hi):
        index = (chan_rank - step) % chan_count
        return lax.dynamic_slice_in_dim(w_full, index * width + lo, hi - lo, axis=2)

    qkv = jnp.einsum("cgd,td->cgt", block_of(0, 0, width), tokens, preferred_element_type=jnp.float32)
    for step, lo, hi, piece in chan_pieces(tokens):
        qkv = qkv + jnp.einsum(
            "cgd,td->cgt", block_of(step, lo, hi), piece, preferred_element_type=jnp.float32
        )
    qkv_b = qkv.astype(jnp.bfloat16)
    taps_n = short_taps.shape[0]
    rim_rows = qkv_b[:, :, tok_rows - (taps_n - 1) :]
    prior = from_behind(rim_rows, "seq", 1)
    extended = lax.optimization_barrier(jnp.concatenate([prior, qkv_b], axis=2)).astype(jnp.float32)
    taps = short_taps.transpose(2, 1, 0)
    feat = jnp.zeros((ch_dev, 3, tok_rows), jnp.float32)
    for j in range(taps_n):
        feat = (
            feat
            + taps[:, :, j : j + 1] * extended[:, :, taps_n - 1 - j : taps_n - 1 - j + tok_rows]
        )
    query = feat[:, 0]
    zprod = (feat[:, 1] * feat[:, 2]).astype(jnp.bfloat16)
    z_f = lax.optimization_barrier(zprod).astype(jnp.float32)
    gains = residue * jnp.sqrt(decay)
    tau = jnp.arange(tok_rows, dtype=jnp.float32)
    grow, fall, tail, onward = lax.optimization_barrier(
        (
            jnp.exp(decay[:, :, None] * tau),
            jnp.exp(-decay[:, :, None] * tau),
            jnp.exp(-decay[:, :, None] * (tok_rows - 1.0 - tau)),
            jnp.exp(-decay[:, :, None] * (tau + 1.0)),
        )
    )
    upper = (tau[:, None] <= tau[None, :]).astype(jnp.bfloat16)
    ending = jnp.sum(tail * z_f[None], axis=2)
    states = lax.all_to_all(
        jnp.broadcast_to(ending[None], (seq_count,) + ending.shape),
        "seq",
        split_axis=0,
        concat_axis=0,
        tiled=True,
    )
    blocks = jnp.arange(seq_count)
    lag = jnp.maximum(seq_rank - 1 - blocks, 0).astype(jnp.float32)
    carry = jnp.where(
        (blocks < seq_rank)[:, None, None],
        jnp.exp(-decay[None] * (tok_rows * lag)[:, None, None]),
        0.0,
    )
    incoming = jnp.sum(carry * states, axis=0)
    lifted = grow * z_f[None]
    prefix = jnp.zeros_like(lifted)
    for _ in range(3):
        part = lifted.astype(jnp.bfloat16)
        prefix = prefix + jnp.einsum("mcs,st->mct", part, upper, preferred_element_type=jnp.float32)
        lifted = lifted - part.astype(jnp.float32)
    intra = fall * prefix
    near = jnp.sum(gains[:, :, None] * intra, axis=0)
    conv = near + jnp.sum((gains * incoming)[:, :, None] * onward, axis=0)
    longc = (conv + skip[:, None] * z_f).astype(jnp.bfloat16)
    long_f = lax.optimization_barrier(longc).astype(jnp.float32)
    gated = (query * long_f).astype(jnp.bfloat16)
    def rows_of(step):
        index = (chan_rank - step) % chan_count
        return lax.dynamic_slice_in_dim(w_out, index * ch_dev, ch_dev, axis=0)

    shifts = sorted(
        [step if step <= chan_count // 2 else step - chan_count for step in range(1, chan_count)],
        key=lambda step: -abs(step),
    )
    arrived = [(step, ring_shift(gated, "chan", step)) for step in shifts]
    mixed = jnp.einsum("ct,ce->te", gated, rows_of(0), preferred_element_type=jnp.float32)
    for step, piece in arrived:
        mixed = mixed + jnp.einsum(
            "ct,ce->te", piece, rows_of(step), preferred_element_type=jnp.float32
        )
    return mixed.astype(jnp.bfloat16)


def solution(mesh):
    placed = (
        P(("rep", "seq"), "chan"),
        P("chan", None, "seq"),
        P(None, None, "chan"),
        P(None, "chan"),
        P(None, "chan"),
        P("chan"),
        P(None, "chan"),
    )
    return jax.shard_map(
        on_device, mesh=mesh, in_specs=placed, out_specs=P(("rep", "seq"), "chan"), check_vma=False
    )
```

```python
import jax
import jax.numpy as jnp
from jax import lax
from jax.sharding import PartitionSpec as P


def from_behind(value, axis, steps):
    count = lax.axis_size(axis)
    leading, last = (max(0, -steps), min(count, count - steps))
    return lax.ppermute(value, axis, [(source, source + steps) for source in range(leading, last)])


def ring_shift(value, axis, steps):
    count = lax.axis_size(axis)
    return lax.ppermute(value, axis, [(source, (source + steps) % count) for source in range(count)])


def chan_pieces(tokens):
    count = lax.axis_size("chan")
    width = tokens.shape[1]
    if count != 4:
        return [(step, 0, width, ring_shift(tokens, "chan", step)) for step in range(1, count)]
    half = width // 2
    ahead_lo = ring_shift(tokens[:, :half], "chan", 1)
    behind_hi = ring_shift(tokens[:, half:], "chan", -1)
    far_lo = ring_shift(ahead_lo, "chan", 1)
    far_hi = ring_shift(behind_hi, "chan", -1)
    ahead_hi = ring_shift(tokens[:, half:], "chan", 1)
    behind_lo = ring_shift(tokens[:, :half], "chan", -1)
    return [
        (1, 0, half, ahead_lo),
        (-1, half, width, behind_hi),
        (1, half, width, ahead_hi),
        (-1, 0, half, behind_lo),
        (2, 0, half, far_lo),
        (2, half, width, far_hi),
    ]


def on_device(tokens, w_in, short_taps, decay, residue, skip, w_out):
    seq_count = lax.axis_size("seq")
    seq_rank = lax.axis_index("seq")
    chan_count = lax.axis_size("chan")
    chan_rank = lax.axis_index("chan")
    tok_rows = tokens.shape[0]
    width = tokens.shape[1]
    ch_dev = w_in.shape[0]
    w_full = lax.all_gather(w_in, "seq", axis=2, tiled=True)

    def block_of(step, lo, hi):
        index = (chan_rank - step) % chan_count
        return lax.dynamic_slice_in_dim(w_full, index * width + lo, hi - lo, axis=2)

    qkv = jnp.einsum("cgd,td->cgt", block_of(0, 0, width), tokens, preferred_element_type=jnp.float32)
    for step, lo, hi, piece in chan_pieces(tokens):
        qkv = qkv + jnp.einsum(
            "cgd,td->cgt", block_of(step, lo, hi), piece, preferred_element_type=jnp.float32
        )
    qkv_b = qkv.astype(jnp.bfloat16)
    taps_n = short_taps.shape[0]
    rim_rows = qkv_b[:, :, tok_rows - (taps_n - 1) :]
    prior = from_behind(rim_rows, "seq", 1)
    extended = lax.optimization_barrier(jnp.concatenate([prior, qkv_b], axis=2)).astype(jnp.float32)
    taps = short_taps.transpose(2, 1, 0)
    feat = jnp.zeros((ch_dev, 3, tok_rows), jnp.float32)
    for j in range(taps_n):
        feat = (
            feat
            + taps[:, :, j : j + 1] * extended[:, :, taps_n - 1 - j : taps_n - 1 - j + tok_rows]
        )
    query = feat[:, 0]
    zprod = (feat[:, 1] * feat[:, 2]).astype(jnp.bfloat16)
    z_f = lax.optimization_barrier(zprod).astype(jnp.float32)
    gains = residue * jnp.sqrt(decay)
    tau = jnp.arange(tok_rows, dtype=jnp.float32)
    grow = jnp.exp(decay[:, :, None] * tau)
    fall = jnp.exp(-decay[:, :, None] * tau)
    upper = (tau[:, None] <= tau[None, :]).astype(jnp.float32)
    tail = jnp.exp(-decay[:, :, None] * (tok_rows - 1.0 - tau))
    ending = jnp.sum(tail * z_f[None], axis=2)
    states = lax.all_to_all(
        jnp.broadcast_to(ending[None], (seq_count,) + ending.shape),
        "seq",
        split_axis=0,
        concat_axis=0,
        tiled=True,
    )
    blocks = jnp.arange(seq_count)
    lag = jnp.maximum(seq_rank - 1 - blocks, 0).astype(jnp.float32)
    carry = jnp.where(
        (blocks < seq_rank)[:, None, None],
        jnp.exp(-decay[None] * (tok_rows * lag)[:, None, None]),
        0.0,
    )
    incoming = jnp.sum(carry * states, axis=0)
    prefix = jnp.einsum(
        "mcs,st->mct",
        grow * z_f[None],
        upper,
        precision=lax.Precision.HIGH,
        preferred_element_type=jnp.float32,
    )
    intra = fall * prefix
    near = jnp.sum(gains[:, :, None] * intra, axis=0)
    onward = lax.optimization_barrier(jnp.exp(-decay[:, :, None] * (tau + 1.0)))
    conv = near + jnp.sum((gains * incoming)[:, :, None] * onward, axis=0)
    longc = (conv + skip[:, None] * z_f).astype(jnp.bfloat16)
    long_f = lax.optimization_barrier(longc).astype(jnp.float32)
    gated = (query * long_f).astype(jnp.bfloat16)
    def rows_of(step):
        index = (chan_rank - step) % chan_count
        return lax.dynamic_slice_in_dim(w_out, index * ch_dev, ch_dev, axis=0)

    shifts = sorted(
        [step if step <= chan_count // 2 else step - chan_count for step in range(1, chan_count)],
        key=lambda step: -abs(step),
    )
    arrived = [(step, ring_shift(gated, "chan", step)) for step in shifts]
    mixed = jnp.einsum("ct,ce->te", gated, rows_of(0), preferred_element_type=jnp.float32)
    for step, piece in arrived:
        mixed = mixed + jnp.einsum(
            "ct,ce->te", piece, rows_of(step), preferred_element_type=jnp.float32
        )
    return mixed.astype(jnp.bfloat16)


def solution(mesh):
    placed = (
        P(("rep", "seq"), "chan"),
        P("chan", None, "seq"),
        P(None, None, "chan"),
        P(None, "chan"),
        P(None, "chan"),
        P("chan"),
        P(None, "chan"),
    )
    return jax.shard_map(
        on_device, mesh=mesh, in_specs=placed, out_specs=P(("rep", "seq"), "chan"), check_vma=False
    )
```

```python
import jax
import jax.numpy as jnp
from jax import lax
from jax.sharding import PartitionSpec as P


def from_behind(value, axis, steps):
    count = lax.axis_size(axis)
    leading, last = (max(0, -steps), min(count, count - steps))
    return lax.ppermute(value, axis, [(source, source + steps) for source in range(leading, last)])


def ring_shift(value, axis, steps):
    count = lax.axis_size(axis)
    return lax.ppermute(value, axis, [(source, (source + steps) % count) for source in range(count)])


def chan_pieces(tokens):
    count = lax.axis_size("chan")
    width = tokens.shape[1]
    if count != 4:
        return [(step, 0, width, ring_shift(tokens, "chan", step)) for step in range(1, count)]
    half = width // 2
    ahead_lo = ring_shift(tokens[:, :half], "chan", 1)
    behind_hi = ring_shift(tokens[:, half:], "chan", -1)
    far_lo = ring_shift(ahead_lo, "chan", 1)
    far_hi = ring_shift(behind_hi, "chan", -1)
    ahead_hi = ring_shift(tokens[:, half:], "chan", 1)
    behind_lo = ring_shift(tokens[:, :half], "chan", -1)
    return [
        (1, 0, half, ahead_lo),
        (-1, half, width, behind_hi),
        (1, half, width, ahead_hi),
        (-1, 0, half, behind_lo),
        (2, 0, half, far_lo),
        (2, half, width, far_hi),
    ]


def on_device(tokens, w_in, short_taps, decay, residue, skip, w_out):
    seq_count = lax.axis_size("seq")
    seq_rank = lax.axis_index("seq")
    chan_count = lax.axis_size("chan")
    chan_rank = lax.axis_index("chan")
    tok_rows = tokens.shape[0]
    width = tokens.shape[1]
    ch_dev = w_in.shape[0]
    w_full = lax.all_gather(w_in, "seq", axis=2, tiled=True)

    def block_of(step, lo, hi):
        index = (chan_rank - step) % chan_count
        return lax.dynamic_slice_in_dim(w_full, index * width + lo, hi - lo, axis=2)

    qkv = jnp.einsum("cgd,td->cgt", block_of(0, 0, width), tokens, preferred_element_type=jnp.float32)
    for step, lo, hi, piece in chan_pieces(tokens):
        qkv = qkv + jnp.einsum(
            "cgd,td->cgt", block_of(step, lo, hi), piece, preferred_element_type=jnp.float32
        )
    qkv_b = qkv.astype(jnp.bfloat16)
    taps_n = short_taps.shape[0]
    rim_rows = qkv_b[:, :, tok_rows - (taps_n - 1) :]
    prior = from_behind(rim_rows, "seq", 1)
    extended = lax.optimization_barrier(jnp.concatenate([prior, qkv_b], axis=2)).astype(jnp.float32)
    taps = short_taps.transpose(2, 1, 0)
    feat = jnp.zeros((ch_dev, 3, tok_rows), jnp.float32)
    for j in range(taps_n):
        feat = (
            feat
            + taps[:, :, j : j + 1] * extended[:, :, taps_n - 1 - j : taps_n - 1 - j + tok_rows]
        )
    query = feat[:, 0]
    zprod = (feat[:, 1] * feat[:, 2]).astype(jnp.bfloat16)
    z_f = lax.optimization_barrier(zprod).astype(jnp.float32)
    gains = residue * jnp.sqrt(decay)
    tau = jnp.arange(tok_rows, dtype=jnp.float32)
    grow = jnp.exp(decay[:, :, None] * tau)
    fall = jnp.exp(-decay[:, :, None] * tau)
    upper = (tau[:, None] <= tau[None, :]).astype(jnp.float32)
    tail = jnp.exp(-decay[:, :, None] * (tok_rows - 1.0 - tau))
    ending = jnp.sum(tail * z_f[None], axis=2)
    states = lax.all_to_all(
        jnp.broadcast_to(ending[None], (seq_count,) + ending.shape),
        "seq",
        split_axis=0,
        concat_axis=0,
        tiled=True,
    )
    blocks = jnp.arange(seq_count)
    lag = jnp.maximum(seq_rank - 1 - blocks, 0).astype(jnp.float32)
    carry = jnp.where(
        (blocks < seq_rank)[:, None, None],
        jnp.exp(-decay[None] * (tok_rows * lag)[:, None, None]),
        0.0,
    )
    incoming = jnp.sum(carry * states, axis=0)
    prefix = jnp.einsum(
        "mcs,st->mct",
        grow * z_f[None],
        upper,
        precision=lax.Precision.HIGH,
        preferred_element_type=jnp.float32,
    )
    intra = fall * prefix
    near = jnp.sum(gains[:, :, None] * intra, axis=0)
    onward = lax.optimization_barrier(jnp.exp(-decay[:, :, None] * (tau + 1.0)))
    conv = near + jnp.sum((gains * incoming)[:, :, None] * onward, axis=0)
    longc = (conv + skip[:, None] * z_f).astype(jnp.bfloat16)
    long_f = lax.optimization_barrier(longc).astype(jnp.float32)
    gated = (query * long_f).astype(jnp.bfloat16)
    every = lax.all_to_all(
        jnp.broadcast_to(gated[None], (chan_count,) + gated.shape),
        "chan",
        split_axis=0,
        concat_axis=0,
        tiled=True,
    )
    mixed = jnp.einsum(
        "ct,ce->te",
        every.reshape(chan_count * ch_dev, tok_rows),
        w_out,
        preferred_element_type=jnp.float32,
    )
    return mixed.astype(jnp.bfloat16)


def solution(mesh):
    placed = (
        P(("rep", "seq"), "chan"),
        P("chan", None, "seq"),
        P(None, None, "chan"),
        P(None, "chan"),
        P(None, "chan"),
        P("chan"),
        P(None, "chan"),
    )
    return jax.shard_map(
        on_device, mesh=mesh, in_specs=placed, out_specs=P(("rep", "seq"), "chan"), check_vma=False
    )
```

```python
import jax
import jax.numpy as jnp
from jax import lax
from jax.sharding import PartitionSpec as P


def from_behind(value, axis, steps):
    count = lax.axis_size(axis)
    leading, last = (max(0, -steps), min(count, count - steps))
    return lax.ppermute(value, axis, [(source, source + steps) for source in range(leading, last)])


def ring_shift(value, axis, steps):
    count = lax.axis_size(axis)
    return lax.ppermute(value, axis, [(source, (source + steps) % count) for source in range(count)])


def chan_pieces(tokens):
    count = lax.axis_size("chan")
    width = tokens.shape[1]
    if count != 4:
        return [(step, 0, width, ring_shift(tokens, "chan", step)) for step in range(1, count)]
    half = width // 2
    ahead_lo = ring_shift(tokens[:, :half], "chan", 1)
    behind_hi = ring_shift(tokens[:, half:], "chan", -1)
    far_lo = ring_shift(ahead_lo, "chan", 1)
    far_hi = ring_shift(behind_hi, "chan", -1)
    ahead_hi = ring_shift(tokens[:, half:], "chan", 1)
    behind_lo = ring_shift(tokens[:, :half], "chan", -1)
    return [
        (1, 0, half, ahead_lo),
        (-1, half, width, behind_hi),
        (1, half, width, ahead_hi),
        (-1, 0, half, behind_lo),
        (2, 0, half, far_lo),
        (2, half, width, far_hi),
    ]


def on_device(tokens, w_in, short_taps, decay, residue, skip, w_out):
    seq_count = lax.axis_size("seq")
    seq_rank = lax.axis_index("seq")
    chan_count = lax.axis_size("chan")
    chan_rank = lax.axis_index("chan")
    tok_rows = tokens.shape[0]
    width = tokens.shape[1]
    ch_dev = w_in.shape[0]
    w_full = lax.all_gather(w_in, "seq", axis=2, tiled=True)

    def block_of(step, lo, hi):
        index = (chan_rank - step) % chan_count
        return lax.dynamic_slice_in_dim(w_full, index * width + lo, hi - lo, axis=2)

    qkv = jnp.einsum("cgd,td->cgt", block_of(0, 0, width), tokens, preferred_element_type=jnp.float32)
    for step, lo, hi, piece in chan_pieces(tokens):
        qkv = qkv + jnp.einsum(
            "cgd,td->cgt", block_of(step, lo, hi), piece, preferred_element_type=jnp.float32
        )
    qkv_b = qkv.astype(jnp.bfloat16)
    taps_n = short_taps.shape[0]
    rim_rows = qkv_b[:, :, tok_rows - (taps_n - 1) :]
    prior = from_behind(rim_rows, "seq", 1)
    extended = lax.optimization_barrier(jnp.concatenate([prior, qkv_b], axis=2)).astype(jnp.float32)
    taps = short_taps.transpose(2, 1, 0)
    feat = jnp.zeros((ch_dev, 3, tok_rows), jnp.float32)
    for j in range(taps_n):
        feat = (
            feat
            + taps[:, :, j : j + 1] * extended[:, :, taps_n - 1 - j : taps_n - 1 - j + tok_rows]
        )
    query = feat[:, 0]
    zprod = (feat[:, 1] * feat[:, 2]).astype(jnp.bfloat16)
    z_f = lax.optimization_barrier(zprod).astype(jnp.float32)
    gains = residue * jnp.sqrt(decay)
    tau = jnp.arange(tok_rows, dtype=jnp.float32)
    grow = jnp.exp(decay[:, :, None] * tau)
    fall = jnp.exp(-decay[:, :, None] * tau)
    upper = (tau[:, None] <= tau[None, :]).astype(jnp.float32)
    lifted = grow * z_f[None]
    ending = jnp.exp(-decay * (tok_rows - 1.0)) * jnp.sum(lifted, axis=2)
    states = lax.all_to_all(
        jnp.broadcast_to(ending[None], (seq_count,) + ending.shape),
        "seq",
        split_axis=0,
        concat_axis=0,
        tiled=True,
    )
    blocks = jnp.arange(seq_count)
    lag = jnp.maximum(seq_rank - 1 - blocks, 0).astype(jnp.float32)
    carry = jnp.where(
        (blocks < seq_rank)[:, None, None],
        jnp.exp(-decay[None] * (tok_rows * lag)[:, None, None]),
        0.0,
    )
    incoming = jnp.sum(carry * states, axis=0)
    prefix = jnp.einsum(
        "mcs,st->mct",
        lifted,
        upper,
        precision=lax.Precision.HIGH,
        preferred_element_type=jnp.float32,
    )
    intra = fall * prefix
    near = jnp.sum(gains[:, :, None] * intra, axis=0)
    onward = lax.optimization_barrier(jnp.exp(-decay[:, :, None] * (tau + 1.0)))
    conv = near + jnp.sum((gains * incoming)[:, :, None] * onward, axis=0)
    longc = (conv + skip[:, None] * z_f).astype(jnp.bfloat16)
    long_f = lax.optimization_barrier(longc).astype(jnp.float32)
    gated = (query * long_f).astype(jnp.bfloat16)
    def rows_of(step):
        index = (chan_rank - step) % chan_count
        return lax.dynamic_slice_in_dim(w_out, index * ch_dev, ch_dev, axis=0)

    shifts = sorted(
        [step if step <= chan_count // 2 else step - chan_count for step in range(1, chan_count)],
        key=lambda step: -abs(step),
    )
    arrived = [(step, ring_shift(gated, "chan", step)) for step in shifts]
    mixed = jnp.einsum("ct,ce->te", gated, rows_of(0), preferred_element_type=jnp.float32)
    for step, piece in arrived:
        mixed = mixed + jnp.einsum(
            "ct,ce->te", piece, rows_of(step), preferred_element_type=jnp.float32
        )
    return mixed.astype(jnp.bfloat16)


def solution(mesh):
    placed = (
        P(("rep", "seq"), "chan"),
        P("chan", None, "seq"),
        P(None, None, "chan"),
        P(None, "chan"),
        P(None, "chan"),
        P("chan"),
        P(None, "chan"),
    )
    return jax.shard_map(
        on_device, mesh=mesh, in_specs=placed, out_specs=P(("rep", "seq"), "chan"), check_vma=False
    )
```

```python
import jax
import jax.numpy as jnp
from jax import lax
from jax.sharding import PartitionSpec as P


def from_behind(value, axis, steps):
    count = lax.axis_size(axis)
    leading, last = (max(0, -steps), min(count, count - steps))
    return lax.ppermute(value, axis, [(source, source + steps) for source in range(leading, last)])


def ring_shift(value, axis, steps):
    count = lax.axis_size(axis)
    return lax.ppermute(value, axis, [(source, (source + steps) % count) for source in range(count)])


def chan_pieces(tokens):
    count = lax.axis_size("chan")
    width = tokens.shape[1]
    if count != 4:
        return [(step, 0, width, ring_shift(tokens, "chan", step)) for step in range(1, count)]
    half = width // 2
    ahead_lo = ring_shift(tokens[:, :half], "chan", 1)
    behind_hi = ring_shift(tokens[:, half:], "chan", -1)
    far_lo = ring_shift(ahead_lo, "chan", 1)
    far_hi = ring_shift(behind_hi, "chan", -1)
    ahead_hi = ring_shift(tokens[:, half:], "chan", 1)
    behind_lo = ring_shift(tokens[:, :half], "chan", -1)
    return [
        (1, 0, half, ahead_lo),
        (-1, half, width, behind_hi),
        (1, half, width, ahead_hi),
        (-1, 0, half, behind_lo),
        (2, 0, half, far_lo),
        (2, half, width, far_hi),
    ]


def on_device(tokens, w_in, short_taps, decay, residue, skip, w_out):
    seq_count = lax.axis_size("seq")
    seq_rank = lax.axis_index("seq")
    chan_count = lax.axis_size("chan")
    chan_rank = lax.axis_index("chan")
    tok_rows = tokens.shape[0]
    width = tokens.shape[1]
    ch_dev = w_in.shape[0]
    w_full = lax.all_gather(w_in, "seq", axis=2, tiled=True)

    def block_of(step, lo, hi):
        index = (chan_rank - step) % chan_count
        return lax.dynamic_slice_in_dim(w_full, index * width + lo, hi - lo, axis=2)

    qkv = jnp.einsum("cgd,td->cgt", block_of(0, 0, width), tokens, preferred_element_type=jnp.float32)
    for step, lo, hi, piece in chan_pieces(tokens):
        qkv = qkv + jnp.einsum(
            "cgd,td->cgt", block_of(step, lo, hi), piece, preferred_element_type=jnp.float32
        )
    qkv_b = qkv.astype(jnp.bfloat16)
    taps_n = short_taps.shape[0]
    rim_rows = qkv_b[:, :, tok_rows - (taps_n - 1) :]
    prior = from_behind(rim_rows, "seq", 1)
    extended = lax.optimization_barrier(jnp.concatenate([prior, qkv_b], axis=2)).astype(jnp.float32)
    taps = short_taps.transpose(2, 1, 0)
    feat = jnp.zeros((ch_dev, 3, tok_rows), jnp.float32)
    for j in range(taps_n):
        feat = (
            feat
            + taps[:, :, j : j + 1] * extended[:, :, taps_n - 1 - j : taps_n - 1 - j + tok_rows]
        )
    query = feat[:, 0]
    zprod = (feat[:, 1] * feat[:, 2]).astype(jnp.bfloat16)
    z_f = lax.optimization_barrier(zprod).astype(jnp.float32)
    gains = residue * jnp.sqrt(decay)
    tau = jnp.arange(tok_rows, dtype=jnp.float32)
    grow = jnp.exp(decay[:, :, None] * tau)
    fall = jnp.exp(-decay[:, :, None] * tau)
    upper = (tau[:, None] <= tau[None, :]).astype(jnp.float32)
    lifted = grow * z_f[None]
    ending = jnp.exp(-decay * (tok_rows - 1.0)) * jnp.sum(lifted, axis=2)
    states = lax.all_to_all(
        jnp.broadcast_to(ending[None], (seq_count,) + ending.shape),
        "seq",
        split_axis=0,
        concat_axis=0,
        tiled=True,
    )
    blocks = jnp.arange(seq_count)
    lag = jnp.maximum(seq_rank - 1 - blocks, 0).astype(jnp.float32)
    carry = jnp.where(
        (blocks < seq_rank)[:, None, None],
        jnp.exp(-decay[None] * (tok_rows * lag)[:, None, None]),
        0.0,
    )
    incoming = jnp.sum(carry * states, axis=0)
    prefix = jnp.einsum(
        "mcs,st->mct",
        lifted,
        upper,
        precision=lax.Precision.HIGH,
        preferred_element_type=jnp.float32,
    )
    intra = fall * prefix
    near = jnp.sum(gains[:, :, None] * intra, axis=0)
    near, incoming = lax.optimization_barrier((near, incoming))
    onward = lax.optimization_barrier(jnp.exp(-decay[:, :, None] * (tau + 1.0)))
    conv = near + jnp.sum((gains * incoming)[:, :, None] * onward, axis=0)
    longc = (conv + skip[:, None] * z_f).astype(jnp.bfloat16)
    long_f = lax.optimization_barrier(longc).astype(jnp.float32)
    gated = (query * long_f).astype(jnp.bfloat16)
    def rows_of(step):
        index = (chan_rank - step) % chan_count
        return lax.dynamic_slice_in_dim(w_out, index * ch_dev, ch_dev, axis=0)

    shifts = sorted(
        [step if step <= chan_count // 2 else step - chan_count for step in range(1, chan_count)],
        key=lambda step: -abs(step),
    )
    arrived = [(step, ring_shift(gated, "chan", step)) for step in shifts]
    mixed = jnp.einsum("ct,ce->te", gated, rows_of(0), preferred_element_type=jnp.float32)
    for step, piece in arrived:
        mixed = mixed + jnp.einsum(
            "ct,ce->te", piece, rows_of(step), preferred_element_type=jnp.float32
        )
    return mixed.astype(jnp.bfloat16)


def solution(mesh):
    placed = (
        P(("rep", "seq"), "chan"),
        P("chan", None, "seq"),
        P(None, None, "chan"),
        P(None, "chan"),
        P(None, "chan"),
        P("chan"),
        P(None, "chan"),
    )
    return jax.shard_map(
        on_device, mesh=mesh, in_specs=placed, out_specs=P(("rep", "seq"), "chan"), check_vma=False
    )
```
